512 devices in a mesh: doc: 16 (over z_lo, y), label: 32 (over x, z_hi, core).
Axes of the slice: x: 4, y: 8, z: 8 (z_hi: 4, z_lo: 2; z = z_hi * 2 + z_lo), core: 2. Of those that a mesh axis runs over, the one named last changes fastest.
Arguments:
- doc_embed: bfloat16 [16384, 768], P(('doc', 'label')), may hold values from -0.59765625 to 0.59765625
- classifier: bfloat16 [32768, 768], P('label'), may hold values from -4.28125 to 4.28125
- centroids: bfloat16 [256, 768], P('doc'), may hold values from -4.28125 to 4.28125
- shortlist: int32 [16384, 32], P(('doc', 'label')), may hold values from 0 to 255, all different within a row
- positives: int32 [16384, 4], P(('doc', 'label')), may hold values from 0 to 4095
Outputs:
- grad_classifier: bfloat16 [32768, 768], P('label')
- grad_centroids: float32 [256, 768], P('doc')
- grad_docs: bfloat16 [16384, 768], P(('doc', 'label'))
The draws below stay inside these ranges and needn't reach their ends.
Inputs may be any that keep to these rules, and one draw needn't show every extreme that they name: `shortlist`: each row names 32 different clusters; every cluster is named by some row.
All inputs are finite; a program needn't handle non-finite values.
Results may differ from the reference program's by a relative error of at most 0.015.
Values may be sent and summed in bfloat16 or wider, within the bound.
No kernel may reach another device: no remote copies, remote signals or barrier semaphores. Data moves between devices by JAX's collectives and lax.ppermute only.
A program may use at most 64 MiB of HBM per device.

```python
import jax
import jax.numpy as jnp
from jax import lax

D = 768
CLS = 128
CL_LAB = 8
DOC_DEV = 32
SHORT = 32
POS = 4
CLUSTERS = 256
LABELS = 32768
DOCS = 16384
N_DOC = 16
N_LABEL = 32


def set_ends(entries, rng, low, top_value):
    extent = entries.shape
    place = [jax.random.randint(jax.random.fold_in(rng, axis), (), 0, extent[axis]) for axis in range(len(extent))]
    entries = entries.at[tuple(place)].set(low)
    longest = extent.index(max(extent))
    place[longest] = (place[longest] + 1) % extent[longest]
    return entries.at[tuple(place)].set(top_value)


def level_of(own_key, dims, cuts, least, high):
    def one(axis_at, blocks):
        draws = jax.random.uniform(jax.random.fold_in(jax.random.fold_in(own_key, 6), axis_at), (blocks,), jnp.float32, least / len(cuts), high / len(cuts))
        return jnp.repeat(jnp.exp(draws), dims[axis_at] // blocks).reshape((-1,) + (1,) * (len(dims) - axis_at - 1))

    loudness = one(*cuts[0])
    for cut in cuts[1:]:
        loudness = loudness * one(*cut)
    return loudness


def picks_of(stream_key, rows, amount, top, lift):
    ranking = jax.random.permutation(jax.random.fold_in(stream_key, 1), amount)
    favour = ranking
    for power in range(3):
        favour = favour * favour // amount
    favour = favour * lift // amount
    tickets = jax.random.randint(jax.random.fold_in(stream_key, 2), (rows, amount), 0, 4096) + favour
    sure = jax.random.permutation(jax.random.fold_in(stream_key, 3), rows)[jnp.arange(amount) % rows]
    tickets = jnp.where(jnp.arange(rows)[:, None] == sure[None, :], 1 << 14, tickets)
    merit = tickets * amount + jnp.arange(amount)
    return lax.top_k(merit.astype(jnp.int32), top)[1].astype(jnp.int32)


def noise(stream_key, dims, spread, most, split=(), held_as=jnp.bfloat16):
    drawn = spread * jax.random.normal(stream_key, dims, jnp.float32)
    if split:
        drawn = drawn * level_of(stream_key, dims, split, -0.22, 0.18)
    return jnp.clip(drawn, -most, most).astype(held_as)


def setup_inputs(seed: int = 0) -> dict:
    splits = jax.random.split(jax.random.key(seed), 6)
    doc_embed = noise(splits[0], (DOCS, D), 0.1, 0.59765625, ((0, 512),))
    classifier = noise(splits[1], (LABELS, D), 0.72, 4.28125, ((0, 32),))
    centroids = noise(splits[2], (CLUSTERS, D), 0.72, 4.28125, ((0, 16),))
    shortlist = picks_of(splits[3], DOCS, CLUSTERS, SHORT, 2048)
    positives = set_ends(jax.random.randint(splits[4], (DOCS, POS), 0, SHORT * CLS), jax.random.fold_in(splits[4], 1), 0, (SHORT * CLS) - 1).astype(jnp.int32)
    return dict(doc_embed=doc_embed, classifier=classifier, centroids=centroids, shortlist=shortlist, positives=positives)


LOSS_WEIGHT = 0.125


def reference(doc_embed, classifier, centroids, shortlist, positives):
    pos_cluster = jnp.take_along_axis(shortlist, (positives // CLS).astype(jnp.int32), axis=1)
    pos_label = pos_cluster * CLS + positives % CLS
    cluster_ids = jnp.arange(CLUSTERS, dtype=jnp.int32)
    label_ids = jnp.arange(LABELS, dtype=jnp.int32)
    group = DOC_DEV * N_LABEL
    labels_dev = CL_LAB * CLS
    weights_blocks = classifier.astype(jnp.float32).reshape(N_LABEL, labels_dev, D)
    cent_blocks = centroids.astype(jnp.float32).reshape(N_LABEL, CL_LAB, D)

    def one_group(carry, index):
        class_sum, cent_sum = carry
        start = (index * group).astype(jnp.int32)
        rows = lax.dynamic_slice_in_dim(doc_embed, start, group, 0)
        short_rows = lax.dynamic_slice_in_dim(shortlist, start, group, 0)
        pos_rows = lax.dynamic_slice_in_dim(pos_label, start, group, 0)
        pcl_rows = lax.dynamic_slice_in_dim(pos_cluster, start, group, 0)
        meta_logits = jnp.dot(rows, centroids.T, preferred_element_type=jnp.float32)
        meta_target = jnp.any(pcl_rows[:, :, None] == cluster_ids[None, None, :], axis=1)
        meta_grad = (LOSS_WEIGHT * (jax.nn.sigmoid(meta_logits) - meta_target.astype(jnp.float32))).astype(jnp.bfloat16)
        cent_part = jnp.dot(meta_grad.T, rows, preferred_element_type=jnp.float32)
        logits = jnp.dot(rows, classifier.T, preferred_element_type=jnp.float32)
        member = jnp.any(short_rows[:, :, None] == cluster_ids[None, None, :], axis=1)
        mask = jnp.repeat(member, CLS, axis=1)
        target = jnp.any(pos_rows[:, :, None] == label_ids[None, None, :], axis=1)
        grad = (LOSS_WEIGHT * (jax.nn.sigmoid(logits) - target.astype(jnp.float32)) * mask.astype(jnp.float32)).astype(jnp.bfloat16)
        class_part = jnp.dot(grad.T, rows, preferred_element_type=jnp.float32).astype(jnp.bfloat16)
        parts = jnp.einsum("nla,lad->lnd", grad.astype(jnp.float32).reshape(group, N_LABEL, labels_dev), weights_blocks)
        parts = parts + jnp.einsum("nlc,lcd->lnd", meta_grad.astype(jnp.float32).reshape(group, N_LABEL, CL_LAB), cent_blocks)
        input_sum = jnp.sum(parts.astype(jnp.bfloat16).astype(jnp.float32), axis=0)
        return (class_sum + class_part.astype(jnp.float32), cent_sum + cent_part), input_sum

    start_carry = (jnp.zeros((LABELS, D), jnp.float32), jnp.zeros((CLUSTERS, D), jnp.float32))
    sums, inputs = lax.scan(one_group, start_carry, jnp.arange(N_DOC, dtype=jnp.int32))
    grad_docs = inputs.reshape(DOCS, D).astype(jnp.bfloat16)
    return sums[0].astype(jnp.bfloat16), sums[1], grad_docs
```

```python
import jax
import jax.numpy as jnp
from jax import lax
from jax.sharding import PartitionSpec as P


CLS = 128
LOSS_WEIGHT = 0.125


def step(doc_embed, classifier, centroids, shortlist, positives):
    n_doc = lax.axis_size("doc")
    labels_dev, width = classifier.shape
    cl_here = labels_dev // CLS
    per_doc = centroids.shape[0]
    docs_dev, short = shortlist.shape
    n_pos = positives.shape[1]
    label_index = lax.axis_index("label")
    cluster_base = label_index * cl_here

    pos_cluster = jnp.take_along_axis(shortlist, positives // CLS, axis=1)
    ints = jnp.concatenate([shortlist, pos_cluster, positives % CLS], axis=1).astype(jnp.bfloat16)
    pad = (-(width + ints.shape[1])) % 128
    packed = jnp.concatenate(
        [doc_embed, ints, jnp.zeros((docs_dev, pad), jnp.bfloat16)], axis=1
    )
    gathered = lax.all_gather(packed, "label", axis=0, tiled=True)
    all_cent = lax.all_gather(centroids, "doc", axis=0, tiled=True)
    gathered, all_cent = lax.optimization_barrier((gathered, all_cent))
    rows = gathered[:, :width]
    ints_rows = gathered[:, width : width + short + 2 * n_pos].astype(jnp.int32)
    short_rows = ints_rows[:, :short]
    pcl_rows = ints_rows[:, short : short + n_pos]
    pos_rows = pcl_rows * CLS + ints_rows[:, short + n_pos :]

    n_clusters = all_cent.shape[0]

    local_clusters = cluster_base + jnp.arange(cl_here, dtype=jnp.int32)
    local_labels = cluster_base * CLS + jnp.arange(labels_dev, dtype=jnp.int32)
    logits = jnp.einsum("nd,ld->nl", rows, classifier, preferred_element_type=jnp.float32)
    member = jnp.any(short_rows[:, :, None] == local_clusters[None, None, :], axis=1)
    mask = jnp.repeat(member, CLS, axis=1)
    target = jnp.any(pos_rows[:, :, None] == local_labels[None, None, :], axis=1)
    grad = (
        LOSS_WEIGHT
        * (jax.nn.sigmoid(logits) - target.astype(jnp.float32))
        * mask.astype(jnp.float32)
    ).astype(jnp.bfloat16)

    docs_part = jnp.dot(grad, classifier, preferred_element_type=jnp.float32).astype(jnp.bfloat16)
    docs_sum = lax.psum_scatter(docs_part, "label", scatter_dimension=0, tiled=True)

    meta_logits = jnp.einsum("nd,cd->nc", rows, all_cent, preferred_element_type=jnp.float32)
    cluster_ids = jnp.arange(n_clusters, dtype=jnp.int32)
    meta_target = jnp.any(pcl_rows[:, :, None] == cluster_ids[None, None, :], axis=1)
    meta_grad = (
        LOSS_WEIGHT * (jax.nn.sigmoid(meta_logits) - meta_target.astype(jnp.float32))
    ).astype(jnp.bfloat16)
    cent_part = jnp.einsum("nc,nd->cd", meta_grad, rows, preferred_element_type=jnp.float32)
    cent_hi = cent_part.astype(jnp.bfloat16)
    cent_lo = (cent_part - cent_hi.astype(jnp.float32)).astype(jnp.bfloat16)

    class_part = jnp.einsum("nl,nd->ld", grad, rows, preferred_element_type=jnp.float32).astype(jnp.bfloat16)
    sub = labels_dev // n_doc
    send = jnp.concatenate(
        [
            class_part.reshape(n_doc, sub, width),
            cent_hi.reshape(n_doc, per_doc, width),
            cent_lo.reshape(n_doc, per_doc, width),
        ],
        axis=1,
    ).reshape(n_doc * (sub + 2 * per_doc), width)
    recv = lax.all_to_all(send, "doc", 0, 0, tiled=True)
    recv = recv.reshape(n_doc, sub + 2 * per_doc, width)
    class_sum = jnp.sum(recv[:, :sub].astype(jnp.float32), axis=0).astype(jnp.bfloat16)
    grad_centroids = jnp.sum(
        recv[:, sub : sub + per_doc].astype(jnp.float32)
        + recv[:, sub + per_doc :].astype(jnp.float32),
        axis=0,
    )
    spread = jnp.broadcast_to(class_sum[None], (n_doc, sub, width)).reshape(n_doc * sub, width)
    grad_classifier = lax.all_to_all(spread, "doc", 0, 0, tiled=True)

    local_meta = lax.dynamic_slice_in_dim(meta_grad, label_index * docs_dev, docs_dev, 0)
    meta_term = jnp.dot(local_meta, all_cent, preferred_element_type=jnp.float32)
    grad_docs = (docs_sum.astype(jnp.float32) + meta_term).astype(jnp.bfloat16)
    return (grad_classifier, grad_centroids, grad_docs)


def solution(mesh):
    in_specs = (
        P(("doc", "label"), None),
        P("label", None),
        P("doc", None),
        P(("doc", "label"), None),
        P(("doc", "label"), None),
    )
    out_specs = (P("label", None), P("doc", None), P(("doc", "label"), None))
    return jax.shard_map(step, mesh=mesh, in_specs=in_specs, out_specs=out_specs, check_vma=False)
```

```python
import jax
import jax.numpy as jnp
from jax import lax
from jax.sharding import PartitionSpec as P


CLS = 128
LOSS_WEIGHT = 0.125


def step(doc_embed, classifier, centroids, shortlist, positives):
    n_doc = lax.axis_size("doc")
    labels_dev, width = classifier.shape
    cl_here = labels_dev // CLS
    per_doc = centroids.shape[0]
    docs_dev, short = shortlist.shape
    n_pos = positives.shape[1]
    label_index = lax.axis_index("label")
    cluster_base = label_index * cl_here

    pos_cluster = jnp.take_along_axis(shortlist, positives // CLS, axis=1)
    ints = jnp.concatenate([shortlist, pos_cluster, positives % CLS], axis=1).astype(jnp.bfloat16)
    pad = (-(width + ints.shape[1])) % 128
    packed = jnp.concatenate(
        [doc_embed, ints, jnp.zeros((docs_dev, pad), jnp.bfloat16)], axis=1
    )
    gathered = lax.all_gather(packed, "label", axis=0, tiled=True)
    all_cent = lax.all_gather(centroids, "doc", axis=0, tiled=True)
    gathered, all_cent = lax.optimization_barrier((gathered, all_cent))
    rows = gathered[:, :width]
    ints_rows = gathered[:, width : width + short + 2 * n_pos].astype(jnp.int32)
    short_rows = ints_rows[:, :short]
    pcl_rows = ints_rows[:, short : short + n_pos]
    pos_rows = pcl_rows * CLS + ints_rows[:, short + n_pos :]

    n_clusters = all_cent.shape[0]

    local_clusters = cluster_base + jnp.arange(cl_here, dtype=jnp.int32)
    logits = jnp.einsum("nd,ld->nl", rows, classifier, preferred_element_type=jnp.float32)
    member = jnp.any(short_rows[:, :, None] == local_clusters[None, None, :], axis=1)
    pos_local = pos_rows - cluster_base * CLS
    label_ids = jnp.arange(labels_dev, dtype=jnp.int32).reshape(1, cl_here, CLS)
    target = pos_local[:, 0, None, None] == label_ids
    for p in range(1, n_pos):
        target = target | (pos_local[:, p, None, None] == label_ids)
    grad = (
        LOSS_WEIGHT
        * (jax.nn.sigmoid(logits.reshape(-1, cl_here, CLS)) - target.astype(jnp.float32))
        * member[:, :, None].astype(jnp.float32)
    ).astype(jnp.bfloat16).reshape(-1, labels_dev)

    docs_part = jnp.dot(grad, classifier, preferred_element_type=jnp.float32).astype(jnp.bfloat16)
    docs_sum = lax.psum_scatter(docs_part, "label", scatter_dimension=0, tiled=True)

    meta_logits = jnp.einsum("nd,cd->nc", rows, all_cent, preferred_element_type=jnp.float32)
    cluster_ids = jnp.arange(n_clusters, dtype=jnp.int32)
    meta_target = pcl_rows[:, 0, None] == cluster_ids[None, :]
    for p in range(1, n_pos):
        meta_target = meta_target | (pcl_rows[:, p, None] == cluster_ids[None, :])
    meta_grad = (
        LOSS_WEIGHT * (jax.nn.sigmoid(meta_logits) - meta_target.astype(jnp.float32))
    ).astype(jnp.bfloat16)
    cent_part = jnp.einsum("nc,nd->cd", meta_grad, rows, preferred_element_type=jnp.float32)
    cent_hi = cent_part.astype(jnp.bfloat16)

    class_part = jnp.einsum("nl,nd->ld", grad, rows, preferred_element_type=jnp.float32).astype(jnp.bfloat16)
    sub = labels_dev // n_doc
    send = jnp.concatenate(
        [
            class_part.reshape(n_doc, sub, width),
            cent_hi.reshape(n_doc, per_doc, width),
        ],
        axis=1,
    ).reshape(n_doc * (sub + per_doc), width)
    recv = lax.all_to_all(send, "doc", 0, 0, tiled=True)
    recv = recv.reshape(n_doc, sub + per_doc, width)
    class_sum = jnp.sum(recv[:, :sub].astype(jnp.float32), axis=0).astype(jnp.bfloat16)
    grad_centroids = jnp.sum(recv[:, sub:].astype(jnp.float32), axis=0)
    spread = jnp.broadcast_to(class_sum[None], (n_doc, sub, width)).reshape(n_doc * sub, width)
    grad_classifier = lax.all_to_all(spread, "doc", 0, 0, tiled=True)

    local_meta = lax.dynamic_slice_in_dim(meta_grad, label_index * docs_dev, docs_dev, 0)
    meta_term = jnp.dot(local_meta, all_cent, preferred_element_type=jnp.float32)
    grad_docs = (docs_sum.astype(jnp.float32) + meta_term).astype(jnp.bfloat16)
    return (grad_classifier, grad_centroids, grad_docs)


def solution(mesh):
    in_specs = (
        P(("doc", "label"), None),
        P("label", None),
        P("doc", None),
        P(("doc", "label"), None),
        P(("doc", "label"), None),
    )
    out_specs = (P("label", None), P("doc", None), P(("doc", "label"), None))
    return jax.shard_map(step, mesh=mesh, in_specs=in_specs, out_specs=out_specs, check_vma=False)
```

```python
import jax
import jax.numpy as jnp
from jax import lax
from jax.sharding import PartitionSpec as P


CLS = 128
LOSS_WEIGHT = 0.125


def step(doc_embed, classifier, centroids, shortlist, positives):
    n_doc = lax.axis_size("doc")
    labels_dev, width = classifier.shape
    cl_here = labels_dev // CLS
    per_doc = centroids.shape[0]
    docs_dev, short = shortlist.shape
    n_pos = positives.shape[1]
    label_index = lax.axis_index("label")
    cluster_base = label_index * cl_here

    n_label = lax.axis_size("label")
    pos_cluster = jnp.take_along_axis(shortlist, positives // CLS, axis=1)
    ints = jnp.concatenate([shortlist, pos_cluster, positives % CLS], axis=1)
    ints_rows = lax.all_to_all(
        jnp.broadcast_to(ints[None], (n_label,) + ints.shape).reshape(n_label * docs_dev, -1),
        "label", 0, 0, tiled=True,
    )
    all_cent = lax.all_to_all(
        jnp.broadcast_to(centroids[None], (n_doc,) + centroids.shape).reshape(n_doc * per_doc, width),
        "doc", 0, 0, tiled=True,
    )
    n_clusters = all_cent.shape[0]
    short_rows = ints_rows[:, :short]
    pcl_rows = ints_rows[:, short : short + n_pos]
    pos_local = pcl_rows * CLS + ints_rows[:, short + n_pos :] - cluster_base * CLS
    local_clusters = cluster_base + jnp.arange(cl_here, dtype=jnp.int32)
    member = jnp.any(short_rows[:, :, None] == local_clusters[None, None, :], axis=1)
    member = member.astype(jnp.float32)

    rows = lax.all_gather(doc_embed, "label", axis=0, tiled=True)
    rows, all_cent, member, pos_local, pcl_rows = lax.optimization_barrier(
        (rows, all_cent, member, pos_local, pcl_rows)
    )

    logits = jnp.einsum("nd,ld->nl", rows, classifier, preferred_element_type=jnp.float32)
    label_ids = jnp.arange(labels_dev, dtype=jnp.int32).reshape(1, cl_here, CLS)
    target = pos_local[:, 0, None, None] == label_ids
    for p in range(1, n_pos):
        target = target | (pos_local[:, p, None, None] == label_ids)
    grad = (
        LOSS_WEIGHT
        * (jax.nn.sigmoid(logits.reshape(-1, cl_here, CLS)) - target.astype(jnp.float32))
        * member[:, :, None]
    ).astype(jnp.bfloat16).reshape(-1, labels_dev)

    docs_part = jnp.dot(grad, classifier, preferred_element_type=jnp.float32).astype(jnp.bfloat16)
    docs_sum = lax.psum_scatter(docs_part, "label", scatter_dimension=0, tiled=True)

    meta_logits = jnp.einsum("nd,cd->nc", rows, all_cent, preferred_element_type=jnp.float32)
    cluster_ids = jnp.arange(n_clusters, dtype=jnp.int32)
    meta_target = pcl_rows[:, 0, None] == cluster_ids[None, :]
    for p in range(1, n_pos):
        meta_target = meta_target | (pcl_rows[:, p, None] == cluster_ids[None, :])
    meta_grad = (
        LOSS_WEIGHT * (jax.nn.sigmoid(meta_logits) - meta_target.astype(jnp.float32))
    ).astype(jnp.bfloat16)
    cent_part = jnp.einsum("nc,nd->cd", meta_grad, rows, preferred_element_type=jnp.float32)
    cent_hi = cent_part.astype(jnp.bfloat16)

    class_part = jnp.einsum("nl,nd->ld", grad, rows, preferred_element_type=jnp.float32).astype(jnp.bfloat16)
    sub = labels_dev // n_doc
    send = jnp.concatenate(
        [
            class_part.reshape(n_doc, sub, width),
            cent_hi.reshape(n_doc, per_doc, width),
        ],
        axis=1,
    ).reshape(n_doc * (sub + per_doc), width)
    recv = lax.all_to_all(send, "doc", 0, 0, tiled=True)
    recv = recv.reshape(n_doc, sub + per_doc, width)
    class_sum = jnp.sum(recv[:, :sub].astype(jnp.float32), axis=0).astype(jnp.bfloat16)
    grad_centroids = jnp.sum(recv[:, sub:].astype(jnp.float32), axis=0)
    spread = jnp.broadcast_to(class_sum[None], (n_doc, sub, width)).reshape(n_doc * sub, width)
    grad_classifier = lax.all_to_all(spread, "doc", 0, 0, tiled=True)

    local_meta = lax.dynamic_slice_in_dim(meta_grad, label_index * docs_dev, docs_dev, 0)
    meta_term = jnp.dot(local_meta, all_cent, preferred_element_type=jnp.float32)
    grad_docs = (docs_sum.astype(jnp.float32) + meta_term).astype(jnp.bfloat16)
    return (grad_classifier, grad_centroids, grad_docs)


def solution(mesh):
    in_specs = (
        P(("doc", "label"), None),
        P("label", None),
        P("doc", None),
        P(("doc", "label"), None),
        P(("doc", "label"), None),
    )
    out_specs = (P("label", None), P("doc", None), P(("doc", "label"), None))
    return jax.shard_map(step, mesh=mesh, in_specs=in_specs, out_specs=out_specs, check_vma=False)
```

```python
import jax
import jax.numpy as jnp
from jax import lax
from jax.sharding import PartitionSpec as P


CLS = 128
LOSS_WEIGHT = 0.125


def step(doc_embed, classifier, centroids, shortlist, positives):
    n_doc = lax.axis_size("doc")
    labels_dev, width = classifier.shape
    cl_here = labels_dev // CLS
    per_doc = centroids.shape[0]
    docs_dev, short = shortlist.shape
    n_pos = positives.shape[1]
    label_index = lax.axis_index("label")
    cluster_base = label_index * cl_here

    n_label = lax.axis_size("label")
    pos_cluster = jnp.take_along_axis(shortlist, positives // CLS, axis=1)
    ints = jnp.concatenate([shortlist, pos_cluster, positives % CLS], axis=1)
    ints_rows = lax.all_to_all(
        jnp.broadcast_to(ints[None], (n_label,) + ints.shape).reshape(n_label * docs_dev, -1),
        "label", 0, 0, tiled=True,
    )
    all_cent = lax.all_to_all(
        jnp.broadcast_to(centroids[None], (n_doc,) + centroids.shape).reshape(n_doc * per_doc, width),
        "doc", 0, 0, tiled=True,
    )
    n_clusters = all_cent.shape[0]
    short_rows = ints_rows[:, :short]
    pcl_rows = ints_rows[:, short : short + n_pos]
    pos_local = pcl_rows * CLS + ints_rows[:, short + n_pos :] - cluster_base * CLS
    local_clusters = cluster_base + jnp.arange(cl_here, dtype=jnp.int32)
    member = jnp.any(short_rows[:, :, None] == local_clusters[None, None, :], axis=1)
    member = member.astype(jnp.float32)

    rows = lax.all_gather(doc_embed, "label", axis=0, tiled=True)
    rows, all_cent, member, pos_local, pcl_rows = lax.optimization_barrier(
        (rows, all_cent, member, pos_local, pcl_rows)
    )

    logits = jnp.einsum("nd,ld->nl", rows, classifier, preferred_element_type=jnp.float32)
    label_ids = jnp.arange(labels_dev, dtype=jnp.int32).reshape(1, cl_here, CLS)
    target = pos_local[:, 0, None, None] == label_ids
    for p in range(1, n_pos):
        target = target | (pos_local[:, p, None, None] == label_ids)
    grad = (
        LOSS_WEIGHT
        * (jax.nn.sigmoid(logits.reshape(-1, cl_here, CLS)) - target.astype(jnp.float32))
        * member[:, :, None]
    ).astype(jnp.bfloat16).reshape(-1, labels_dev)

    docs_part = jnp.dot(grad, classifier, preferred_element_type=jnp.float32).astype(jnp.bfloat16)
    docs_sum = lax.psum_scatter(docs_part, "label", scatter_dimension=0, tiled=True)

    meta_logits = jnp.einsum("nd,cd->nc", rows, all_cent, preferred_element_type=jnp.float32)
    cluster_ids = jnp.arange(n_clusters, dtype=jnp.int32)
    meta_target = pcl_rows[:, 0, None] == cluster_ids[None, :]
    for p in range(1, n_pos):
        meta_target = meta_target | (pcl_rows[:, p, None] == cluster_ids[None, :])
    meta_grad = (
        LOSS_WEIGHT * (jax.nn.sigmoid(meta_logits) - meta_target.astype(jnp.float32))
    ).astype(jnp.bfloat16)
    cent_part = jnp.einsum("nc,nd->cd", meta_grad, rows, preferred_element_type=jnp.float32)
    half = per_doc // 2
    parity = label_index % 2
    cent_mine = lax.dynamic_slice_in_dim(
        cent_part.reshape(n_doc, 2, half, width), parity, 1, 1
    ).astype(jnp.bfloat16)

    class_part = jnp.einsum("nl,nd->ld", grad, rows, preferred_element_type=jnp.float32).astype(jnp.bfloat16)
    sub = labels_dev // n_doc
    send = jnp.concatenate(
        [class_part.reshape(n_doc, sub, width), cent_mine.reshape(n_doc, half, width)],
        axis=1,
    ).reshape(n_doc * (sub + half), width)
    recv = lax.all_to_all(send, "doc", 0, 0, tiled=True)
    recv = recv.reshape(n_doc, sub + half, width)
    class_sum = jnp.sum(recv[:, :sub].astype(jnp.float32), axis=0).astype(jnp.bfloat16)
    cent_sum = jnp.sum(recv[:, sub:].astype(jnp.float32), axis=0)
    n_label = lax.axis_size("label")
    cent_other = lax.ppermute(cent_sum, "label", [(i, i ^ 1) for i in range(n_label)])
    grad_centroids = jnp.where(
        parity == 0,
        jnp.concatenate([cent_sum, cent_other], axis=0),
        jnp.concatenate([cent_other, cent_sum], axis=0),
    )
    spread = jnp.broadcast_to(class_sum[None], (n_doc, sub, width)).reshape(n_doc * sub, width)
    gathered_class = lax.all_to_all(spread, "doc", 0, 0, tiled=True)
    grad_classifier = jnp.where(parity >= 0, gathered_class, jnp.zeros_like(gathered_class))

    local_meta = lax.dynamic_slice_in_dim(meta_grad, label_index * docs_dev, docs_dev, 0)
    meta_term = jnp.dot(local_meta, all_cent, preferred_element_type=jnp.float32)
    grad_docs = (docs_sum.astype(jnp.float32) + meta_term).astype(jnp.bfloat16)
    return (grad_classifier, grad_centroids, grad_docs)


def solution(mesh):
    in_specs = (
        P(("doc", "label"), None),
        P("label", None),
        P("doc", None),
        P(("doc", "label"), None),
        P(("doc", "label"), None),
    )
    out_specs = (P("label", None), P("doc", None), P(("doc", "label"), None))
    return jax.shard_map(step, mesh=mesh, in_specs=in_specs, out_specs=out_specs, check_vma=False)
```

```python
import jax
import jax.numpy as jnp
from jax import lax
from jax.sharding import PartitionSpec as P


CLS = 128
LOSS_WEIGHT = 0.125


def step(doc_embed, classifier, centroids, shortlist, positives):
    n_doc = lax.axis_size("doc")
    labels_dev, width = classifier.shape
    cl_here = labels_dev // CLS
    per_doc = centroids.shape[0]
    docs_dev, short = shortlist.shape
    n_pos = positives.shape[1]
    label_index = lax.axis_index("label")
    cluster_base = label_index * cl_here

    n_label = lax.axis_size("label")
    pos_cluster = jnp.take_along_axis(shortlist, positives // CLS, axis=1)
    ints = jnp.concatenate([shortlist, pos_cluster, positives % CLS], axis=1)
    ints_rows = lax.all_to_all(
        jnp.broadcast_to(ints[None], (n_label,) + ints.shape).reshape(n_label * docs_dev, -1),
        "label", 0, 0, tiled=True,
    )
    all_cent = lax.all_to_all(
        jnp.broadcast_to(centroids[None], (n_doc,) + centroids.shape).reshape(n_doc * per_doc, width),
        "doc", 0, 0, tiled=True,
    )
    n_clusters = all_cent.shape[0]
    short_rows = ints_rows[:, :short]
    pcl_rows = ints_rows[:, short : short + n_pos]
    pos_local = pcl_rows * CLS + ints_rows[:, short + n_pos :] - cluster_base * CLS
    local_clusters = cluster_base + jnp.arange(cl_here, dtype=jnp.int32)
    member = jnp.any(short_rows[:, :, None] == local_clusters[None, None, :], axis=1)
    member = member.astype(jnp.bfloat16)

    rows = lax.all_gather(doc_embed, "label", axis=0, tiled=True)
    rows, all_cent, member, pos_local, pcl_rows = lax.optimization_barrier(
        (rows, all_cent, member, pos_local, pcl_rows)
    )

    logits = jnp.einsum("nd,ld->nl", rows, classifier, preferred_element_type=jnp.float32)
    label_ids = jnp.arange(labels_dev, dtype=jnp.int32).reshape(1, cl_here, CLS)
    target = pos_local[:, 0, None, None] == label_ids
    for p in range(1, n_pos):
        target = target | (pos_local[:, p, None, None] == label_ids)
    grad = (
        (LOSS_WEIGHT * (jax.nn.sigmoid(logits.reshape(-1, cl_here, CLS)) - target.astype(jnp.float32)))
        .astype(jnp.bfloat16)
        * member[:, :, None]
    ).reshape(-1, labels_dev)

    docs_part = jnp.dot(grad, classifier, preferred_element_type=jnp.float32).astype(jnp.bfloat16)
    docs_sum = lax.psum_scatter(docs_part, "label", scatter_dimension=0, tiled=True)

    meta_logits = jnp.einsum("nd,cd->nc", rows, all_cent, preferred_element_type=jnp.float32)
    cluster_ids = jnp.arange(n_clusters, dtype=jnp.int32)
    meta_target = pcl_rows[:, 0, None] == cluster_ids[None, :]
    for p in range(1, n_pos):
        meta_target = meta_target | (pcl_rows[:, p, None] == cluster_ids[None, :])
    meta_grad = (
        LOSS_WEIGHT * (jax.nn.sigmoid(meta_logits) - meta_target.astype(jnp.float32))
    ).astype(jnp.bfloat16)
    cent_part = jnp.einsum("nc,nd->cd", meta_grad, rows, preferred_element_type=jnp.float32)
    half = per_doc // 2
    parity = label_index % 2
    cent_mine = lax.dynamic_slice_in_dim(
        cent_part.reshape(n_doc, 2, half, width), parity, 1, 1
    ).astype(jnp.bfloat16)

    class_part = jnp.einsum("nl,nd->ld", grad, rows, preferred_element_type=jnp.float32).astype(jnp.bfloat16)
    sub = labels_dev // n_doc
    send = jnp.concatenate(
        [class_part.reshape(n_doc, sub, width), cent_mine.reshape(n_doc, half, width)],
        axis=1,
    ).reshape(n_doc * (sub + half), width)
    recv = lax.all_to_all(send, "doc", 0, 0, tiled=True)
    recv = recv.reshape(n_doc, sub + half, width)
    class_sum = jnp.sum(recv[:, :sub].astype(jnp.float32), axis=0).astype(jnp.bfloat16)
    cent_sum = jnp.sum(recv[:, sub:].astype(jnp.float32), axis=0)
    n_label = lax.axis_size("label")
    cent_other = lax.ppermute(cent_sum, "label", [(i, i ^ 1) for i in range(n_label)])
    grad_centroids = jnp.where(
        parity == 0,
        jnp.concatenate([cent_sum, cent_other], axis=0),
        jnp.concatenate([cent_other, cent_sum], axis=0),
    )
    spread = jnp.broadcast_to(class_sum[None], (n_doc, sub, width)).reshape(n_doc * sub, width)
    gathered_class = lax.all_to_all(spread, "doc", 0, 0, tiled=True)
    grad_classifier = jnp.where(parity >= 0, gathered_class, jnp.zeros_like(gathered_class))

    local_meta = lax.dynamic_slice_in_dim(meta_grad, label_index * docs_dev, docs_dev, 0)
    meta_term = jnp.dot(local_meta, all_cent, preferred_element_type=jnp.float32)
    grad_docs = (docs_sum.astype(jnp.float32) + meta_term).astype(jnp.bfloat16)
    return (grad_classifier, grad_centroids, grad_docs)


def solution(mesh):
    in_specs = (
        P(("doc", "label"), None),
        P("label", None),
        P("doc", None),
        P(("doc", "label"), None),
        P(("doc", "label"), None),
    )
    out_specs = (P("label", None), P("doc", None), P(("doc", "label"), None))
    return jax.shard_map(step, mesh=mesh, in_specs=in_specs, out_specs=out_specs, check_vma=False)
```
